256 devices in a mesh: space: 64 (over y, z, core), pa: 2 (over x_lo), pb: 2 (over x_hi).
Axes of the slice: x: 4 (x_hi: 2, x_lo: 2; x = x_hi * 2 + x_lo), y: 4, z: 8, core: 2. Of those that a mesh axis runs over, the one named last changes fastest.
Arguments:
- field: float32 [8192, 16, 16, 16, 16], P('space', 'pa', None, 'pb'), may hold values from -6 to 6
- g_first: float32 [16, 128], P('pa'), may hold values from -1.5 to 1.5
- g_second: float32 [16, 128], replicated, may hold values from -1.5 to 1.5
- g_third: float32 [16, 128], P('pb'), may hold values from -1.5 to 1.5
- g_fourth: float32 [16, 128], replicated, may hold values from -1.5 to 1.5
- h_second: float32 [16, 128], replicated, may hold values from -1.5 to 1.5
- h_third: float32 [16, 128], P('pb'), may hold values from -1.5 to 1.5
- h_fourth: float32 [16, 128], replicated, may hold values from -1.5 to 1.5
Outputs:
- basis: float32 [8192, 128], P('space')
- core: float32 [128, 16, 16, 16, 16], P('space', 'pa', None, 'pb')
- next_sketch: float32 [128, 16, 128], P('space', 'pa')
The draws below stay inside these ranges and needn't reach their ends.
All inputs are finite; a program needn't handle non-finite values.
Results may differ from the reference program's by a relative error of at most 0.00011.
Values sent between devices are 32-bit elements; how exact they have to be, the bound alone decides.
No kernel may reach another device: no remote copies, remote signals or barrier semaphores. Data moves between devices by JAX's collectives and lax.ppermute only.
A program may use at most 128 MiB of HBM per device.

```python
import jax
import jax.numpy as jnp
from jax import lax

MODE = 16
RANK = 128
POINTS = 8192


def shard_levels(rng, shape, pieces, least, top_value):
    factor_of, own = 1.0, jax.random.fold_in(rng, 6)
    for axis_at, parts in pieces:
        draws = jnp.exp(jax.random.uniform(jax.random.fold_in(own, axis_at), (parts,), jnp.float32, least / len(pieces), top_value / len(pieces)))
        factor_of = factor_of * jnp.repeat(draws, shape[axis_at] // parts).reshape([-1 if axis == axis_at else 1 for axis in range(len(shape))])
    return factor_of


def centred(stream_key, shape, width, most, cuts=(), dtype=jnp.bfloat16):
    array = jax.random.normal(stream_key, shape, jnp.float32) * width
    if len(cuts) > 0:
        array = shard_levels(stream_key, shape, cuts, -0.22, 0.18) * array
    return jnp.clip(array, min=-most, max=most).astype(dtype)


def setup_inputs(seed: int = 0) -> dict:
    key_of = jax.random.split(jax.random.key(seed), 9)
    field = centred(key_of[0], (POINTS, MODE, MODE, MODE, MODE), 1.0, 6.0, ((0, 64), (1, 2), (3, 2)), jnp.float32)
    g_first = centred(key_of[1], (MODE, RANK), MODE ** -0.5, 1.5, ((0, 2),), jnp.float32)
    g_second = centred(key_of[2], (MODE, RANK), MODE ** -0.5, 1.5, (), jnp.float32)
    g_third = centred(key_of[3], (MODE, RANK), MODE ** -0.5, 1.5, ((0, 2),), jnp.float32)
    g_fourth = centred(key_of[4], (MODE, RANK), MODE ** -0.5, 1.5, (), jnp.float32)
    h_second = centred(key_of[5], (MODE, RANK), MODE ** -0.5, 1.5, (), jnp.float32)
    h_third = centred(key_of[6], (MODE, RANK), MODE ** -0.5, 1.5, ((0, 2),), jnp.float32)
    h_fourth = centred(key_of[7], (MODE, RANK), MODE ** -0.5, 1.5, (), jnp.float32)
    return dict(field=field, g_first=g_first, g_second=g_second, g_third=g_third, g_fourth=g_fourth, h_second=h_second, h_third=h_third, h_fourth=h_fourth)


def reference(field, g_first, g_second, g_third, g_fourth, h_second, h_third, h_fourth):
    highest = lax.Precision.HIGHEST
    flat = field.reshape(POINTS, MODE ** 4)
    omega = (g_first[:, None, None, None, :] * g_second[None, :, None, None, :] * g_third[None, None, :, None, :] * g_fourth[None, None, None, :, :]).reshape(MODE ** 4, RANK)
    sketch = jnp.dot(flat.astype(jnp.float32), omega.astype(jnp.float32), precision=highest, preferred_element_type=jnp.float32)
    gram = jnp.dot(sketch.T.astype(jnp.float32), sketch.astype(jnp.float32), precision=highest, preferred_element_type=jnp.float32)
    lower = jnp.linalg.cholesky(gram)
    basis = lax.linalg.triangular_solve(lower, sketch, left_side=False, lower=True, transpose_a=True)
    core = jnp.dot(basis.T.astype(jnp.float32), flat.astype(jnp.float32), precision=highest, preferred_element_type=jnp.float32)
    psi = (h_second[:, None, None, :] * h_third[None, :, None, :] * h_fourth[None, None, :, :]).reshape(MODE ** 3, RANK)
    next_sketch = jnp.dot(core.reshape(RANK * MODE, MODE ** 3).astype(jnp.float32), psi.astype(jnp.float32), precision=highest, preferred_element_type=jnp.float32)
    return (basis, core.reshape(RANK, MODE, MODE, MODE, MODE), next_sketch.reshape(RANK, MODE, RANK))
```

```python
import jax
import numpy as np
import jax.numpy as jnp
from jax import lax
from jax.sharding import PartitionSpec as P

MODE = 16
RANK = 128


def butterfly_sum(x, axis, size):
    step = 1
    while step < size:
        x = x + lax.ppermute(x, axis, [(i, i ^ step) for i in range(size)])
        step *= 2
    return x


def bit_reverse(value, bits):
    out = 0
    for _ in range(bits):
        out = (out << 1) | (value & 1)
        value >>= 1
    return out


def halving_scatter(x, axis, size):
    idx = lax.axis_index(axis)
    step = 1
    while step < size:
        half = x.shape[0] // 2
        bit = (idx // step) % 2
        keep = lax.dynamic_slice_in_dim(x, bit * half, half, 0)
        send = lax.dynamic_slice_in_dim(x, (1 - bit) * half, half, 0)
        x = keep + lax.ppermute(send, axis, [(i, i ^ step) for i in range(size)])
        step *= 2
    return x


def body(field, g_first, g_second, g_third, g_fourth, h_second, h_third, h_fourth, *, n_space, n_pa, n_pb):
    highest = lax.Precision.HIGHEST
    rows = field.shape[0]
    first_loc = field.shape[1]
    third_loc = field.shape[3]
    width = first_loc * MODE * third_loc * MODE
    flat = field.reshape(rows, width)
    omega = (
        g_first[:, None, None, None, :]
        * g_second[None, :, None, None, :]
        * g_third[None, None, :, None, :]
        * g_fourth[None, None, None, :, :]
    ).reshape(width, RANK)
    partial_sketch = jnp.dot(flat, omega, precision=highest, preferred_element_type=jnp.float32)
    sketch = butterfly_sum(butterfly_sum(partial_sketch, "pa", n_pa), "pb", n_pb)
    gram = butterfly_sum(
        jnp.dot(sketch.T, sketch, precision=highest, preferred_element_type=jnp.float32), "space", n_space
    )
    lower = jnp.linalg.cholesky(gram)
    basis = lax.linalg.triangular_solve(
        lower, sketch, left_side=False, lower=True, transpose_a=True
    )
    bits = n_space.bit_length() - 1
    per = RANK // n_space
    order = np.array([per * bit_reverse(b, bits) + t for b in range(n_space) for t in range(per)])
    core_flat = halving_scatter(
        lax.dot_general(
            basis[:, order],
            flat,
            (((0,), (0,)), ((), ())),
            precision=highest,
            preferred_element_type=jnp.float32,
        ),
        "space",
        n_space,
    )
    own_rank = core_flat.shape[0]
    psi = (
        h_second[:, None, None, :] * h_third[None, :, None, :] * h_fourth[None, None, :, :]
    ).reshape(MODE * third_loc * MODE, RANK)
    partial_next = jnp.dot(
        core_flat.reshape(own_rank * first_loc, MODE * third_loc * MODE),
        psi,
        precision=highest,
        preferred_element_type=jnp.float32,
    )
    next_sketch = butterfly_sum(partial_next, "pb", n_pb)
    core = core_flat.reshape(own_rank, first_loc, MODE, third_loc, MODE)
    return (basis, core, next_sketch.reshape(own_rank, first_loc, RANK))


def solution(mesh):
    placed = (
        P("space", "pa", None, "pb", None),
        P("pa", None),
        P(),
        P("pb", None),
        P(),
        P(),
        P("pb", None),
        P(),
    )
    sizes = dict(n_space=mesh.shape["space"], n_pa=mesh.shape["pa"], n_pb=mesh.shape["pb"])
    return jax.shard_map(
        lambda *a: body(*a, **sizes),
        mesh=mesh,
        in_specs=placed,
        out_specs=(P("space", None), P("space", "pa", None, "pb", None), P("space", "pa", None)),
        check_vma=False,
    )
```

```python
import jax
import numpy as np
import jax.numpy as jnp
from jax import lax
from jax.sharding import PartitionSpec as P

MODE = 16
RANK = 128


def butterfly_sum(x, axis, size):
    step = 1
    while step < size:
        if step * 4 <= size:
            near = lax.ppermute(x, axis, [(i, i ^ step) for i in range(size)])
            far = lax.ppermute(x, axis, [(i, i ^ (2 * step)) for i in range(size)])
            farther = lax.ppermute(x, axis, [(i, i ^ (3 * step)) for i in range(size)])
            x = (x + near) + (far + farther)
            step *= 4
        else:
            x = x + lax.ppermute(x, axis, [(i, i ^ step) for i in range(size)])
            step *= 2
    return x


def scatter_steps(size):
    if size == 64:
        return {0: (1, 2, 16, 4, 32, 8), 1: (1, 16, 2, 32, 4, 8)}
    plain = tuple(1 << k for k in range(size.bit_length() - 1))
    return {0: plain, 1: plain}


def scatter_layout(size, per):
    steps = scatter_steps(size)
    rounds = len(steps[0])
    table = np.zeros((size, size * per), np.int32)
    for d in range(size):
        for b in range(size):
            seq = steps[b & 1]
            pos = 0
            for r, st in enumerate(seq):
                pos |= (((b ^ d) // st) % 2) << (rounds - 1 - r)
            for t in range(per):
                table[d, pos * per + t] = b * per + t
    return table


def halving_scatter(x, axis, size):
    steps = scatter_steps(size)
    for r in range(len(steps[0])):
        half = x.shape[0] // 2
        perm = [(i, i ^ steps[i & 1][r]) for i in range(size)]
        x = x[:half] + lax.ppermute(x[half:], axis, perm)
    return x


def body(field, g_first, g_second, g_third, g_fourth, h_second, h_third, h_fourth, *, n_space, n_pa, n_pb):
    highest = lax.Precision.HIGHEST
    rows = field.shape[0]
    first_loc = field.shape[1]
    third_loc = field.shape[3]
    width = first_loc * MODE * third_loc * MODE
    flat = field.reshape(rows, width)
    omega = (
        g_first[:, None, None, None, :]
        * g_second[None, :, None, None, :]
        * g_third[None, None, :, None, :]
        * g_fourth[None, None, None, :, :]
    ).reshape(width, RANK)
    partial_sketch = jnp.dot(flat, omega, precision=highest, preferred_element_type=jnp.float32)
    sketch = butterfly_sum(partial_sketch, ("pa", "pb"), n_pa * n_pb)
    gram = butterfly_sum(
        jnp.dot(sketch.T, sketch, precision=highest, preferred_element_type=jnp.float32), "space", n_space
    )
    lower = jnp.linalg.cholesky(gram)
    basis = lax.linalg.triangular_solve(
        lower, sketch, left_side=False, lower=True, transpose_a=True
    )
    per = RANK // n_space
    order = jnp.asarray(scatter_layout(n_space, per))[lax.axis_index("space")]
    core_flat = halving_scatter(
        lax.dot_general(
            jnp.take(basis, order, axis=1),
            flat,
            (((0,), (0,)), ((), ())),
            precision=highest,
            preferred_element_type=jnp.float32,
        ),
        "space",
        n_space,
    )
    own_rank = core_flat.shape[0]
    psi = (
        h_second[:, None, None, :] * h_third[None, :, None, :] * h_fourth[None, None, :, :]
    ).reshape(MODE * third_loc * MODE, RANK)
    partial_next = jnp.dot(
        core_flat.reshape(own_rank * first_loc, MODE * third_loc * MODE),
        psi,
        precision=highest,
        preferred_element_type=jnp.float32,
    )
    next_sketch = butterfly_sum(partial_next, "pb", n_pb)
    core = core_flat.reshape(own_rank, first_loc, MODE, third_loc, MODE)
    return (basis, core, next_sketch.reshape(own_rank, first_loc, RANK))


def solution(mesh):
    placed = (
        P("space", "pa", None, "pb", None),
        P("pa", None),
        P(),
        P("pb", None),
        P(),
        P(),
        P("pb", None),
        P(),
    )
    sizes = dict(n_space=mesh.shape["space"], n_pa=mesh.shape["pa"], n_pb=mesh.shape["pb"])
    return jax.shard_map(
        lambda *a: body(*a, **sizes),
        mesh=mesh,
        in_specs=placed,
        out_specs=(P("space", None), P("space", "pa", None, "pb", None), P("space", "pa", None)),
        check_vma=False,
    )
```

```python
import jax
import numpy as np
import jax.numpy as jnp
from jax import lax
from jax.sharding import PartitionSpec as P

MODE = 16
RANK = 128


def butterfly_sum(x, axis, size):
    step = 1
    while step < size:
        if step * 4 <= size:
            near = lax.ppermute(x, axis, [(i, i ^ step) for i in range(size)])
            far = lax.ppermute(x, axis, [(i, i ^ (2 * step)) for i in range(size)])
            farther = lax.ppermute(x, axis, [(i, i ^ (3 * step)) for i in range(size)])
            x = (x + near) + (far + farther)
            step *= 4
        else:
            x = x + lax.ppermute(x, axis, [(i, i ^ step) for i in range(size)])
            step *= 2
    return x


def scatter_steps(size):
    if size == 64:
        return {0: (1, 2, 16, 4, 32, 8), 1: (1, 16, 2, 32, 4, 8)}
    plain = tuple(1 << k for k in range(size.bit_length() - 1))
    return {0: plain, 1: plain}


def scatter_layout(size, per):
    steps = scatter_steps(size)
    rounds = len(steps[0])
    table = np.zeros((size, size * per), np.int32)
    for d in range(size):
        for b in range(size):
            seq = steps[b & 1]
            pos = 0
            for r, st in enumerate(seq):
                pos |= (((b ^ d) // st) % 2) << (rounds - 1 - r)
            for t in range(per):
                table[d, pos * per + t] = b * per + t
    return table


def halving_scatter(x, axis, size):
    steps = scatter_steps(size)
    for r in range(len(steps[0])):
        half = x.shape[0] // 2
        perm = [(i, i ^ steps[i & 1][r]) for i in range(size)]
        x = x[:half] + lax.ppermute(x[half:], axis, perm)
    return x


def body(field, g_first, g_second, g_third, g_fourth, h_second, h_third, h_fourth, *, n_space, n_pa, n_pb):
    highest = lax.Precision.HIGHEST
    rows = field.shape[0]
    first_loc = field.shape[1]
    third_loc = field.shape[3]
    width = first_loc * MODE * third_loc * MODE
    flat = field.reshape(rows, width)
    omega = (
        g_first[:, None, None, None, :]
        * g_second[None, :, None, None, :]
        * g_third[None, None, :, None, :]
        * g_fourth[None, None, None, :, :]
    ).reshape(width, RANK)
    partial_sketch = jnp.dot(flat, omega, precision=lax.Precision.HIGH, preferred_element_type=jnp.float32)
    sketch = butterfly_sum(partial_sketch, ("pa", "pb"), n_pa * n_pb)
    gram = butterfly_sum(
        jnp.dot(sketch.T, sketch, precision=highest, preferred_element_type=jnp.float32), "space", n_space
    )
    lower = jnp.linalg.cholesky(gram)
    basis = lax.linalg.triangular_solve(
        lower, sketch, left_side=False, lower=True, transpose_a=True
    )
    per = RANK // n_space
    order = jnp.asarray(scatter_layout(n_space, per))[lax.axis_index("space")]
    core_flat = halving_scatter(
        lax.dot_general(
            jnp.take(basis, order, axis=1),
            flat,
            (((0,), (0,)), ((), ())),
            precision=lax.Precision.HIGH,
            preferred_element_type=jnp.float32,
        ),
        "space",
        n_space,
    )
    own_rank = core_flat.shape[0]
    psi = (
        h_second[:, None, None, :] * h_third[None, :, None, :] * h_fourth[None, None, :, :]
    ).reshape(MODE * third_loc * MODE, RANK)
    partial_next = jnp.dot(
        core_flat.reshape(own_rank * first_loc, MODE * third_loc * MODE),
        psi,
        precision=highest,
        preferred_element_type=jnp.float32,
    )
    next_sketch = butterfly_sum(partial_next, "pb", n_pb)
    core = core_flat.reshape(own_rank, first_loc, MODE, third_loc, MODE)
    return (basis, core, next_sketch.reshape(own_rank, first_loc, RANK))


def solution(mesh):
    placed = (
        P("space", "pa", None, "pb", None),
        P("pa", None),
        P(),
        P("pb", None),
        P(),
        P(),
        P("pb", None),
        P(),
    )
    sizes = dict(n_space=mesh.shape["space"], n_pa=mesh.shape["pa"], n_pb=mesh.shape["pb"])
    return jax.shard_map(
        lambda *a: body(*a, **sizes),
        mesh=mesh,
        in_specs=placed,
        out_specs=(P("space", None), P("space", "pa", None, "pb", None), P("space", "pa", None)),
        check_vma=False,
    )
```

```python
import jax
import numpy as np
import jax.numpy as jnp
from jax import lax
from jax.sharding import PartitionSpec as P

MODE = 16
RANK = 128


def butterfly_sum(x, axis, size):
    step = 1
    while step < size:
        if step * 4 <= size:
            near = lax.ppermute(x, axis, [(i, i ^ step) for i in range(size)])
            far = lax.ppermute(x, axis, [(i, i ^ (2 * step)) for i in range(size)])
            farther = lax.ppermute(x, axis, [(i, i ^ (3 * step)) for i in range(size)])
            x = (x + near) + (far + farther)
            step *= 4
        else:
            x = x + lax.ppermute(x, axis, [(i, i ^ step) for i in range(size)])
            step *= 2
    return x


def scatter_steps(size):
    if size == 64:
        return {0: (1, 2, 16, 4, 32, 8), 1: (1, 16, 2, 32, 4, 8)}
    plain = tuple(1 << k for k in range(size.bit_length() - 1))
    return {0: plain, 1: plain}


def row_layout(size, per):
    steps = scatter_steps(size)
    table = np.zeros((size, size * per), np.int32)
    for d in range(size):
        seq = steps[d & 1]
        rest = seq[2:]
        for b in range(size):
            pos = 0
            for r, st in enumerate(rest):
                pos |= (((b ^ d) // st) % 2) << (len(rest) - 1 - r)
            w = (b & 1) * 2 + (b // seq[1]) % 2
            for t in range(per):
                table[d, (pos * 4 + w) * per + t] = b * per + t
    return table


def column_round(x, axis, size, r):
    steps = scatter_steps(size)
    idx = lax.axis_index(axis)
    st = jnp.asarray(np.array([steps[0][r], steps[1][r]], np.int32))[idx % 2]
    bit = (idx // st) % 2
    half = x.shape[1] // 2
    keep = lax.dynamic_slice_in_dim(x, bit * half, half, 1)
    send = lax.dynamic_slice_in_dim(x, (1 - bit) * half, half, 1)
    return keep + lax.ppermute(send, axis, [(i, i ^ steps[i & 1][r]) for i in range(size)])


def row_rounds(x, axis, size):
    steps = scatter_steps(size)
    for r in range(2, len(steps[0])):
        half = x.shape[0] // 2
        perm = [(i, i ^ steps[i & 1][r]) for i in range(size)]
        x = x[:half] + lax.ppermute(x[half:], axis, perm)
    return x


def gather_own_rows(x, axis, size, per):
    steps = scatter_steps(size)
    idx = lax.axis_index(axis)
    c = idx % 2
    st2 = jnp.asarray(np.array([steps[0][1], steps[1][1]], np.int32))
    own_st, other_st = st2[c], st2[1 - c]
    j = (idx // own_st) % 2
    j1 = (idx // other_st) % 2

    def rows_of(b):
        w = (b % 2) * 2 + (b // own_st) % 2
        return lax.dynamic_slice_in_dim(x, w * per, per, 0)

    same = lax.ppermute(rows_of(idx ^ own_st), axis, [(i, i ^ steps[i & 1][1]) for i in range(size)])
    pair = lax.ppermute(rows_of(idx ^ 1), axis, [(i, i ^ 1) for i in range(size)])
    cross = lax.ppermute(
        rows_of(idx ^ 1 ^ own_st), axis, [(i, i ^ 1 ^ steps[i & 1][1]) for i in range(size)]
    )
    pieces = jnp.stack([rows_of(idx), same, pair, cross])
    high = jnp.array([0, 0, 1, 1], jnp.int32)
    low = jnp.array([0, 1, 0, 1], jnp.int32)
    src = jnp.where(high == c, jnp.where(low == j, 0, 1), jnp.where(low == j1, 2, 3))
    picked = jnp.take(pieces, src, axis=0)
    return jnp.swapaxes(picked, 0, 1).reshape(per, -1)


def body(field, g_first, g_second, g_third, g_fourth, h_second, h_third, h_fourth, *, n_space, n_pa, n_pb):
    highest = lax.Precision.HIGHEST
    rows = field.shape[0]
    first_loc = field.shape[1]
    third_loc = field.shape[3]
    width = first_loc * MODE * third_loc * MODE
    flat = field.reshape(rows, width)
    omega = (
        g_first[:, None, None, None, :]
        * g_second[None, :, None, None, :]
        * g_third[None, None, :, None, :]
        * g_fourth[None, None, None, :, :]
    ).reshape(width, RANK)
    partial_sketch = jnp.dot(flat, omega, precision=lax.Precision.HIGH, preferred_element_type=jnp.float32)
    sketch = butterfly_sum(partial_sketch, ("pa", "pb"), n_pa * n_pb)
    gram = butterfly_sum(
        jnp.dot(sketch.T, sketch, precision=highest, preferred_element_type=jnp.float32), "space", n_space
    )
    projected = lax.dot_general(
        sketch, flat, (((0,), (0,)), ((), ())), precision=lax.Precision.HIGH, preferred_element_type=jnp.float32
    )
    projected = column_round(column_round(projected, "space", n_space, 0), "space", n_space, 1)
    lower = jnp.linalg.cholesky(gram)
    inverse = lax.linalg.triangular_solve(
        lower, jnp.eye(RANK, dtype=jnp.float32), left_side=True, lower=True
    )
    basis = jnp.dot(sketch, inverse.T, precision=highest, preferred_element_type=jnp.float32)
    per = RANK // n_space
    order = jnp.asarray(row_layout(n_space, per))[lax.axis_index("space")]
    core_part = jnp.dot(
        jnp.take(inverse, order, axis=0), projected, precision=lax.Precision.HIGH, preferred_element_type=jnp.float32
    )
    core_flat = gather_own_rows(row_rounds(core_part, "space", n_space), "space", n_space, per)
    own_rank = core_flat.shape[0]
    psi = (
        h_second[:, None, None, :] * h_third[None, :, None, :] * h_fourth[None, None, :, :]
    ).reshape(MODE * third_loc * MODE, RANK)
    partial_next = jnp.dot(
        core_flat.reshape(own_rank * first_loc, MODE * third_loc * MODE),
        psi,
        precision=highest,
        preferred_element_type=jnp.float32,
    )
    next_sketch = butterfly_sum(partial_next, "pb", n_pb)
    core = core_flat.reshape(own_rank, first_loc, MODE, third_loc, MODE)
    return (basis, core, next_sketch.reshape(own_rank, first_loc, RANK))


def solution(mesh):
    placed = (
        P("space", "pa", None, "pb", None),
        P("pa", None),
        P(),
        P("pb", None),
        P(),
        P(),
        P("pb", None),
        P(),
    )
    sizes = dict(n_space=mesh.shape["space"], n_pa=mesh.shape["pa"], n_pb=mesh.shape["pb"])
    return jax.shard_map(
        lambda *a: body(*a, **sizes),
        mesh=mesh,
        in_specs=placed,
        out_specs=(P("space", None), P("space", "pa", None, "pb", None), P("space", "pa", None)),
        check_vma=False,
    )
```

```python
import jax
import numpy as np
import jax.numpy as jnp
from jax import lax
from jax.sharding import PartitionSpec as P

MODE = 16
RANK = 128


def butterfly_sum(x, axis, size, step=1, stop=None):
    stop = size if stop is None else stop
    while step < stop:
        if step * 4 <= size:
            near = lax.ppermute(x, axis, [(i, i ^ step) for i in range(size)])
            far = lax.ppermute(x, axis, [(i, i ^ (2 * step)) for i in range(size)])
            farther = lax.ppermute(x, axis, [(i, i ^ (3 * step)) for i in range(size)])
            x = (x + near) + (far + farther)
            step *= 4
        else:
            x = x + lax.ppermute(x, axis, [(i, i ^ step) for i in range(size)])
            step *= 2
    return x


def scatter_steps(size):
    if size == 64:
        return {0: (1, 2, 16, 4, 32, 8), 1: (1, 16, 2, 32, 4, 8)}
    plain = tuple(1 << k for k in range(size.bit_length() - 1))
    return {0: plain, 1: plain}


def row_layout(size, per):
    steps = scatter_steps(size)
    table = np.zeros((size, size * per), np.int32)
    for d in range(size):
        seq = steps[d & 1]
        rest = seq[2:]
        for b in range(size):
            pos = 0
            for r, st in enumerate(rest):
                pos |= (((b ^ d) // st) % 2) << (len(rest) - 1 - r)
            w = (b & 1) * 2 + (b // seq[1]) % 2
            for t in range(per):
                table[d, (pos * 4 + w) * per + t] = b * per + t
    return table


def column_round(x, axis, size, r):
    steps = scatter_steps(size)
    idx = lax.axis_index(axis)
    st = jnp.asarray(np.array([steps[0][r], steps[1][r]], np.int32))[idx % 2]
    bit = (idx // st) % 2
    half = x.shape[1] // 2
    keep = lax.dynamic_slice_in_dim(x, bit * half, half, 1)
    send = lax.dynamic_slice_in_dim(x, (1 - bit) * half, half, 1)
    return keep + lax.ppermute(send, axis, [(i, i ^ steps[i & 1][r]) for i in range(size)])


def row_rounds(x, axis, size):
    steps = scatter_steps(size)
    for r in range(2, len(steps[0])):
        half = x.shape[0] // 2
        perm = [(i, i ^ steps[i & 1][r]) for i in range(size)]
        x = x[:half] + lax.ppermute(x[half:], axis, perm)
    return x


def gather_own_rows(x, axis, size, per):
    steps = scatter_steps(size)
    idx = lax.axis_index(axis)
    c = idx % 2
    st2 = jnp.asarray(np.array([steps[0][1], steps[1][1]], np.int32))
    own_st, other_st = st2[c], st2[1 - c]
    j = (idx // own_st) % 2
    j1 = (idx // other_st) % 2

    def rows_of(b):
        w = (b % 2) * 2 + (b // own_st) % 2
        return lax.dynamic_slice_in_dim(x, w * per, per, 0)

    same = lax.ppermute(rows_of(idx ^ own_st), axis, [(i, i ^ steps[i & 1][1]) for i in range(size)])
    pair = lax.ppermute(rows_of(idx ^ 1), axis, [(i, i ^ 1) for i in range(size)])
    cross = lax.ppermute(
        rows_of(idx ^ 1 ^ own_st), axis, [(i, i ^ 1 ^ steps[i & 1][1]) for i in range(size)]
    )
    pieces = jnp.stack([rows_of(idx), same, pair, cross])
    high = jnp.array([0, 0, 1, 1], jnp.int32)
    low = jnp.array([0, 1, 0, 1], jnp.int32)
    src = jnp.where(high == c, jnp.where(low == j, 0, 1), jnp.where(low == j1, 2, 3))
    picked = jnp.take(pieces, src, axis=0)
    return jnp.swapaxes(picked, 0, 1).reshape(per, -1)


def body(field, g_first, g_second, g_third, g_fourth, h_second, h_third, h_fourth, *, n_space, n_pa, n_pb):
    highest = lax.Precision.HIGHEST
    rows = field.shape[0]
    first_loc = field.shape[1]
    third_loc = field.shape[3]
    width = first_loc * MODE * third_loc * MODE
    flat = field.reshape(rows, width)
    omega = (
        g_first[:, None, None, None, :]
        * g_second[None, :, None, None, :]
        * g_third[None, None, :, None, :]
        * g_fourth[None, None, None, :, :]
    ).reshape(width, RANK)
    partial_sketch = jnp.dot(flat, omega, precision=lax.Precision.HIGH, preferred_element_type=jnp.float32)
    sketch = butterfly_sum(partial_sketch, ("pa", "pb"), n_pa * n_pb)
    gram_part = jnp.dot(sketch.T, sketch, precision=highest, preferred_element_type=jnp.float32)
    gram_part = butterfly_sum(gram_part, "space", n_space, 1, 4)
    sketch_late, gram_part = lax.optimization_barrier((sketch, gram_part))
    gram = butterfly_sum(gram_part, "space", n_space, 4)
    projected = lax.dot_general(
        sketch_late, flat, (((0,), (0,)), ((), ())), precision=lax.Precision.HIGH, preferred_element_type=jnp.float32
    )
    projected = column_round(projected, "space", n_space, 0)
    projected, gram = lax.optimization_barrier((projected, gram))
    projected = column_round(projected, "space", n_space, 1)
    lower = jnp.linalg.cholesky(gram)
    inverse = lax.linalg.triangular_solve(
        lower, jnp.eye(RANK, dtype=jnp.float32), left_side=True, lower=True
    )
    basis = jnp.dot(sketch, inverse.T, precision=highest, preferred_element_type=jnp.float32)
    per = RANK // n_space
    order = jnp.asarray(row_layout(n_space, per))[lax.axis_index("space")]
    core_part = jnp.dot(
        jnp.take(inverse, order, axis=0), projected, precision=lax.Precision.HIGH, preferred_element_type=jnp.float32
    )
    core_flat = gather_own_rows(row_rounds(core_part, "space", n_space), "space", n_space, per)
    own_rank = core_flat.shape[0]
    psi = (
        h_second[:, None, None, :] * h_third[None, :, None, :] * h_fourth[None, None, :, :]
    ).reshape(MODE * third_loc * MODE, RANK)
    partial_next = jnp.dot(
        core_flat.reshape(own_rank * first_loc, MODE * third_loc * MODE),
        psi,
        precision=highest,
        preferred_element_type=jnp.float32,
    )
    next_sketch = butterfly_sum(partial_next, "pb", n_pb)
    core = core_flat.reshape(own_rank, first_loc, MODE, third_loc, MODE)
    return (basis, core, next_sketch.reshape(own_rank, first_loc, RANK))


def solution(mesh):
    placed = (
        P("space", "pa", None, "pb", None),
        P("pa", None),
        P(),
        P("pb", None),
        P(),
        P(),
        P("pb", None),
        P(),
    )
    sizes = dict(n_space=mesh.shape["space"], n_pa=mesh.shape["pa"], n_pb=mesh.shape["pb"])
    return jax.shard_map(
        lambda *a: body(*a, **sizes),
        mesh=mesh,
        in_specs=placed,
        out_specs=(P("space", None), P("space", "pa", None, "pb", None), P("space", "pa", None)),
        check_vma=False,
    )
```
